256 devices in a mesh: blk: 64 (over z, y, x_lo), grp: 4 (over x_hi, core).
Axes of the slice: x: 4 (x_hi: 2, x_lo: 2; x = x_hi * 2 + x_lo), y: 4, z: 8, core: 2. Of those that a mesh axis runs over, the one named last changes fastest.
Arguments:
- features: bfloat16 [196608, 2048], P(('blk', 'grp'))
- factors: bfloat16 [196608, 512], P(('blk', 'grp'))
- pivots: int32 [2, 256], replicated, may hold values from 0 to 767, as said below
- owners: int32 [2], replicated, may hold values from 0 to 255, as said below
Outputs:
- embedding: float32 [196608], P(('blk', 'grp'))
- columns: bfloat16 [196608, 512], P(('blk', 'grp'))
- leftover: float32 [196608], P(('blk', 'grp'))
The draws below stay inside these ranges and needn't reach their ends.
Inputs may be any that keep to these rules, and one draw needn't show every extreme that they name: `pivots`: each row holds 256 distinct row numbers from 0 to 767. The 2 owners are distinct devices; one of them is the last device.
All inputs are finite; a program needn't handle non-finite values.
Results may differ from the reference program's by a relative error of at most 0.001.
Values may be sent and summed in bfloat16 or wider, within the bound.
No kernel may reach another device: no remote copies, remote signals or barrier semaphores. Data moves between devices by JAX's collectives and lax.ppermute only.
A program may use at most 64 MiB of HBM per device.

```python
import math
import jax
import jax.numpy as jnp
from jax import lax

F = 2048
PIV = 256
R0 = 512
ROUNDS = 2
S = 768
NSCEN = 196608
N_BLK = 64
N_GRP = 4


def draw_features(key, part):
    kcent, kpick, kwhich, kcoef, knoise, katom = jax.random.split(jax.random.fold_in(key, 11), 6)
    row_count = S * N_BLK * N_GRP
    per_block = max(S // 32, 1)
    cluster_count = N_BLK * per_block
    row_ids = jnp.arange(row_count, dtype=jnp.int32)
    block_numbers = row_ids // (N_GRP * S)
    grp_ids = row_ids // S % N_GRP
    offsets = jax.random.randint(kwhich, (row_count,), 0, 3 * per_block, dtype=jnp.int32)
    cluster = grp_ids * cluster_count + (block_numbers * per_block + offsets) % cluster_count
    selected_atoms = jax.random.randint(kpick, (N_GRP * cluster_count, 8), 0, F, dtype=jnp.int32)
    centres = jax.random.normal(kcent, (N_GRP * cluster_count, F), jnp.float32)
    atoms = jax.random.normal(katom, (F, F), jnp.float32)
    weights = jax.random.normal(kcoef, (row_count, 8), jnp.float32)
    noise = jax.random.normal(knoise, (row_count, F), jnp.float32)
    feat = 4.05 * centres[cluster] + 1.789 * noise
    chosen = selected_atoms[cluster]
    for column in range(8):
        feat = feat + 0.5477 * weights[:, column:column + 1] * atoms[chosen[:, column]]
    return feat.astype(jnp.bfloat16)


def draw_factors(key, part):
    scale_random_key, value_random_key = jax.random.split(jax.random.fold_in(key, 23), 2)
    grand_total = S * N_BLK * N_GRP
    noise_level = jnp.exp(jax.random.uniform(scale_random_key, (grand_total, 1), jnp.float32, math.log(0.01), math.log(0.16)))
    vals = jax.random.uniform(value_random_key, (grand_total, R0), jnp.float32, -1.7320508, 1.7320508)
    return (vals * jnp.sqrt(noise_level / R0)).astype(jnp.bfloat16)


def draw_pivots(key, part):
    rows = []
    for rnd in range(ROUNDS):
        order = jax.random.permutation(jax.random.fold_in(key, 31 + rnd), S)
        rows.append(order[:PIV])
    return jnp.stack(rows).astype(jnp.int32)


def draw_owners(key, part):
    device_count = N_BLK * N_GRP
    others = jax.random.permutation(jax.random.fold_in(key, 47), device_count - 1)[:ROUNDS - 1].astype(jnp.int32)
    picked = jnp.concatenate([others, jnp.full((1,), device_count - 1, dtype=jnp.int32)])
    placing = jax.random.permutation(jax.random.fold_in(key, 53), ROUNDS)
    return picked[placing].astype(jnp.int32)


def setup_inputs(seed: int = 0) -> dict:
    splits = jax.random.split(jax.random.key(seed), 5)
    return {
        "features": draw_features(jax.random.fold_in(splits[4], 71), 0),
        "factors": draw_factors(jax.random.fold_in(splits[4], 71), 0),
        "pivots": draw_pivots(jax.random.fold_in(splits[4], 71), 0),
        "owners": draw_owners(jax.random.fold_in(splits[4], 71), 0),
    }


def squares(block):
    wide = block.astype(jnp.float32)
    return jnp.sum(wide * wide, axis=1)

def kernel_block(left, right, left_sq, right_sq):
    gram = jnp.dot(left.astype(jnp.float32), right.T.astype(jnp.float32), preferred_element_type=jnp.float32)
    dist = left_sq[:, None] + right_sq[None, :] - 2.0 * gram
    return jnp.exp(-dist / (8.0 * F))

def solve_block(piv_x, piv_sq, piv_l):
    schur = kernel_block(piv_x, piv_x, piv_sq, piv_sq) - jnp.dot(piv_l.astype(jnp.float32), piv_l.T.astype(jnp.float32), preferred_element_type=jnp.float32)
    lower = jnp.linalg.cholesky(schur)
    ident = jnp.eye(schur.shape[0], dtype=jnp.float32)
    return lax.linalg.triangular_solve(lower, ident, left_side=True, lower=True)

def apply_block(tx, tsq, tl, piv_x, piv_sq, piv_l, inverse):
    cross = kernel_block(tx, piv_x, tsq, piv_sq) - jnp.dot(tl.astype(jnp.float32), piv_l.T.astype(jnp.float32), preferred_element_type=jnp.float32)
    return jnp.dot(cross.astype(jnp.float32), inverse.T.astype(jnp.float32), precision=lax.Precision.HIGHEST, preferred_element_type=jnp.float32).astype(jnp.bfloat16)

def reference(features, factors, pivots, owners):
    devices = N_BLK * N_GRP
    blocks = features.reshape(N_BLK, N_GRP, S, F)

    def embed_one(index):
        bidx = index // N_GRP
        gidx = index % N_GRP
        own = blocks[bidx, gidx]
        own_sq = squares(own)
        grand_total = jnp.sum(kernel_block(own, own, own_sq, own_sq), axis=1)
        for step in (1, 2):
            other = blocks[(bidx - step) % N_BLK, gidx]
            grand_total = grand_total + jnp.sum(kernel_block(own, other, own_sq, squares(other)), axis=1)
        return grand_total / (3.0 * S)
    embedding = lax.map(embed_one, jnp.arange(devices, dtype=jnp.int32)).reshape(-1)
    flat = features.reshape(devices, S, F)
    current = factors
    newcols = []
    for rnd in range(ROUNDS):
        rows = (owners[rnd] * S + pivots[rnd]).astype(jnp.int32)
        piv_x = features[rows]
        piv_l = current[rows]
        piv_sq = squares(piv_x)
        inverse = solve_block(piv_x, piv_sq, piv_l)
        width = current.shape[1]

        def extend_one(pair):
            return apply_block(pair[0], squares(pair[0]), pair[1], piv_x, piv_sq, piv_l, inverse)
        fresh = lax.map(extend_one, (flat, current.reshape(devices, S, width))).reshape(NSCEN, PIV)
        newcols.append(fresh)
        current = jnp.concatenate([current, fresh], axis=1)
    columns = jnp.concatenate(newcols, axis=1)
    wide = current.astype(jnp.float32)
    leftover = 1.0 - jnp.sum(wide * wide, axis=1)
    return (embedding, columns, leftover)
```

```python
import jax
import jax.numpy as jnp
from jax import lax
from jax.sharding import PartitionSpec as P

F = 2048
ROUNDS = 2


def passed_along(value, axis, steps):
    count = lax.axis_size(axis)
    pairs = [(source, (source + steps) % count) for source in range(count)]
    return lax.ppermute(value, axis, pairs)


def device_index():
    return lax.axis_index("blk") * lax.axis_size("grp") + lax.axis_index("grp")


def picked_rows(block, rows, take):
    selector = (rows[:, None] == jnp.arange(block.shape[0], dtype=rows.dtype)[None, :]) & take
    return jnp.dot(selector.astype(block.dtype), block, preferred_element_type=jnp.float32)


def from_owner(features, factors, rows, owner, after=None):
    take = device_index() == owner
    picked = jnp.concatenate(
        [picked_rows(features, rows, take), picked_rows(factors, rows, take)], axis=1
    )
    if after is not None:
        picked, _ = lax.optimization_barrier((picked, after))
    wide = lax.psum(picked, ("blk", "grp"))
    return wide[:, : features.shape[1]], wide[:, features.shape[1] :]


def squares(block):
    wide = block.astype(jnp.float32)
    return jnp.sum(wide * wide, axis=1)


def kernel_block(left, right, left_sq, right_sq):
    gram = jnp.dot(left, right.T, preferred_element_type=jnp.float32)
    dist = left_sq[:, None] + right_sq[None, :] - 2.0 * gram
    return jnp.exp(-dist / (8.0 * F))


def solve_block(piv_x, piv_sq, piv_l):
    schur = kernel_block(piv_x, piv_x, piv_sq, piv_sq) - jnp.dot(
        piv_l, piv_l.T, preferred_element_type=jnp.float32
    )
    lower = jnp.linalg.cholesky(schur)
    ident = jnp.eye(schur.shape[0], dtype=jnp.float32)
    return lax.linalg.triangular_solve(lower, ident, left_side=True, lower=True)


def apply_block(tx, tsq, tl, piv_x, piv_sq, piv_l, inverse):
    cross = kernel_block(tx, piv_x, tsq, piv_sq) - jnp.dot(
        tl, piv_l.T, preferred_element_type=jnp.float32
    )
    return jnp.dot(
        cross, inverse.T, precision=lax.Precision.HIGHEST, preferred_element_type=jnp.float32
    ).astype(jnp.bfloat16)


def on_device(features, factors, pivots, owners):
    rows = features.shape[0]
    received = []
    for rnd in range(ROUNDS):
        after = received[-1][0] if received else None
        received.append(from_owner(features, factors, pivots[rnd], owners[rnd], after))
    own_sq = squares(features)
    grand_total = jnp.sum(kernel_block(features, features, own_sq, own_sq), axis=1)
    for step in (1, 2):
        carried = passed_along(features, "blk", step)
        grand_total = grand_total + jnp.sum(
            kernel_block(features, carried, own_sq, squares(carried)), axis=1
        )
    embedding = grand_total / (3.0 * rows)
    current = factors
    newcols = []
    blocks_x = []
    block_squared_norms = []
    block_factor_rows = []
    inverses = []
    for rnd in range(ROUNDS):
        piv_x, piv_l = received[rnd]
        piv_sq = squares(piv_x)
        for prior in range(rnd):
            extra = apply_block(
                piv_x,
                piv_sq,
                piv_l,
                blocks_x[prior],
                block_squared_norms[prior],
                block_factor_rows[prior],
                inverses[prior],
            )
            piv_l = jnp.concatenate([piv_l, extra], axis=1)
        inverses.append(solve_block(piv_x, piv_sq, piv_l))
        blocks_x.append(piv_x)
        block_squared_norms.append(piv_sq)
        block_factor_rows.append(piv_l)
    for rnd in range(ROUNDS):
        fresh = apply_block(
            features,
            own_sq,
            current,
            blocks_x[rnd],
            block_squared_norms[rnd],
            block_factor_rows[rnd],
            inverses[rnd],
        )
        newcols.append(fresh)
        current = jnp.concatenate([current, fresh], axis=1)
    columns = jnp.concatenate(newcols, axis=1)
    wide = current.astype(jnp.float32)
    leftover = 1.0 - jnp.sum(wide * wide, axis=1)
    return (embedding, columns, leftover)


def solution(mesh):
    placed = (P(("blk", "grp"), None), P(("blk", "grp"), None), P(), P())
    return jax.shard_map(
        on_device,
        mesh=mesh,
        in_specs=placed,
        out_specs=(P(("blk", "grp")), P(("blk", "grp"), None), P(("blk", "grp"))),
        check_vma=False,
    )
```

```python
import jax
import jax.numpy as jnp
from jax import lax
from jax.sharding import PartitionSpec as P

F = 2048
ROUNDS = 2


def passed_along(value, axis, steps):
    count = lax.axis_size(axis)
    pairs = [(source, (source + steps) % count) for source in range(count)]
    return lax.ppermute(value, axis, pairs)


def device_index():
    return lax.axis_index("blk") * lax.axis_size("grp") + lax.axis_index("grp")


def picked_rows(block, rows, take):
    selector = (rows[:, None] == jnp.arange(block.shape[0], dtype=rows.dtype)[None, :]) & take
    return jnp.dot(selector.astype(block.dtype), block, preferred_element_type=jnp.float32)


def from_owner(features, factors, rows, owner):
    take = device_index() == owner
    return jnp.concatenate(
        [picked_rows(features, rows, take), picked_rows(factors, rows, take)], axis=1
    )


def squares(block):
    wide = block.astype(jnp.float32)
    return jnp.sum(wide * wide, axis=1)


def kernel_block(left, right, left_sq, right_sq):
    gram = jnp.dot(left, right.T, preferred_element_type=jnp.float32)
    dist = left_sq[:, None] + right_sq[None, :] - 2.0 * gram
    return jnp.exp(-dist / (8.0 * F))


def solve_block(piv_x, piv_sq, piv_l):
    schur = kernel_block(piv_x, piv_x, piv_sq, piv_sq) - jnp.dot(
        piv_l, piv_l.T, preferred_element_type=jnp.float32
    )
    lower = jnp.linalg.cholesky(schur)
    ident = jnp.eye(schur.shape[0], dtype=jnp.float32)
    return lax.linalg.triangular_solve(lower, ident, left_side=True, lower=True)


def apply_block(tx, tsq, tl, piv_x, piv_sq, piv_l, inverse):
    cross = kernel_block(tx, piv_x, tsq, piv_sq) - jnp.dot(
        tl, piv_l.T, preferred_element_type=jnp.float32
    )
    return jnp.dot(
        cross, inverse.T, precision=lax.Precision.HIGHEST, preferred_element_type=jnp.float32
    ).astype(jnp.bfloat16)


def on_device(features, factors, pivots, owners):
    rows = features.shape[0]
    picked = [from_owner(features, factors, pivots[rnd], owners[rnd]) for rnd in range(ROUNDS)]
    carried = [passed_along(features, "blk", step) for step in (1, 2)]
    picked, carried = lax.optimization_barrier((picked, carried))
    width = features.shape[1]
    received = []
    for rnd in range(ROUNDS):
        wide = lax.psum(picked[rnd], ("blk", "grp"))
        received.append((wide[:, :width], wide[:, width:]))
    own_sq = squares(features)
    grand_total = jnp.sum(kernel_block(features, features, own_sq, own_sq), axis=1)
    for other in carried:
        grand_total = grand_total + jnp.sum(
            kernel_block(features, other, own_sq, squares(other)), axis=1
        )
    embedding = grand_total / (3.0 * rows)
    current = factors
    newcols = []
    blocks_x = []
    block_squared_norms = []
    block_factor_rows = []
    inverses = []
    for rnd in range(ROUNDS):
        piv_x, piv_l = received[rnd]
        piv_sq = squares(piv_x)
        for prior in range(rnd):
            extra = apply_block(
                piv_x,
                piv_sq,
                piv_l,
                blocks_x[prior],
                block_squared_norms[prior],
                block_factor_rows[prior],
                inverses[prior],
            )
            piv_l = jnp.concatenate([piv_l, extra], axis=1)
        inverses.append(solve_block(piv_x, piv_sq, piv_l))
        blocks_x.append(piv_x)
        block_squared_norms.append(piv_sq)
        block_factor_rows.append(piv_l)
    for rnd in range(ROUNDS):
        fresh = apply_block(
            features,
            own_sq,
            current,
            blocks_x[rnd],
            block_squared_norms[rnd],
            block_factor_rows[rnd],
            inverses[rnd],
        )
        newcols.append(fresh)
        current = jnp.concatenate([current, fresh], axis=1)
    columns = jnp.concatenate(newcols, axis=1)
    wide = current.astype(jnp.float32)
    leftover = 1.0 - jnp.sum(wide * wide, axis=1)
    return (embedding, columns, leftover)


def solution(mesh):
    placed = (P(("blk", "grp"), None), P(("blk", "grp"), None), P(), P())
    return jax.shard_map(
        on_device,
        mesh=mesh,
        in_specs=placed,
        out_specs=(P(("blk", "grp")), P(("blk", "grp"), None), P(("blk", "grp"))),
        check_vma=False,
    )
```

```python
import jax
import jax.numpy as jnp
from jax import lax
from jax.sharding import PartitionSpec as P

F = 2048
ROUNDS = 2


def passed_along(value, axis, steps):
    count = lax.axis_size(axis)
    pairs = [(source, (source + steps) % count) for source in range(count)]
    return lax.ppermute(value, axis, pairs)


def device_index():
    return lax.axis_index("blk") * lax.axis_size("grp") + lax.axis_index("grp")


def picked_rows(block, rows, take):
    selector = (rows[:, None] == jnp.arange(block.shape[0], dtype=rows.dtype)[None, :]) & take
    return jnp.dot(selector.astype(block.dtype), block, preferred_element_type=jnp.float32)


def from_owner(features, factors, rows, owner):
    take = device_index() == owner
    return jnp.concatenate(
        [picked_rows(features, rows, take), picked_rows(factors, rows, take)], axis=1
    ).astype(jnp.bfloat16)


def flip_pairs(bit, count):
    return [(source, source ^ (1 << bit)) for source in range(count)]


def broadcast_sum(value, order):
    axes = ("blk", "grp")
    count = lax.axis_size(axes)
    me = device_index()
    current = value
    for bit in order:
        half = current.shape[0] // 2
        upper = ((me >> bit) & 1) == 1
        keep = jnp.where(upper, current[half:], current[:half])
        send = jnp.where(upper, current[:half], current[half:])
        current = keep + lax.ppermute(send, axes, flip_pairs(bit, count))
    for bit in reversed(order):
        upper = ((me >> bit) & 1) == 1
        other = lax.ppermute(current, axes, flip_pairs(bit, count))
        current = jnp.where(
            upper, jnp.concatenate([other, current]), jnp.concatenate([current, other])
        )
    return current


def bit_order(count):
    bits = count.bit_length() - 1
    near = [0, 2, 3, 5, 1, 4, 6, 7]
    return [b for b in near if b < bits] + list(range(len(near), bits))


def squares(block):
    wide = block.astype(jnp.float32)
    return jnp.sum(wide * wide, axis=1)


def kernel_block(left, right, left_sq, right_sq):
    gram = jnp.dot(left, right.T, preferred_element_type=jnp.float32)
    dist = left_sq[:, None] + right_sq[None, :] - 2.0 * gram
    return jnp.exp(-dist / (8.0 * F))


def solve_block(piv_x, piv_sq, piv_l):
    schur = kernel_block(piv_x, piv_x, piv_sq, piv_sq) - jnp.dot(
        piv_l, piv_l.T, preferred_element_type=jnp.float32
    )
    lower = jnp.linalg.cholesky(schur)
    ident = jnp.eye(schur.shape[0], dtype=jnp.float32)
    return lax.linalg.triangular_solve(lower, ident, left_side=True, lower=True)


def apply_block(tx, tsq, tl, piv_x, piv_sq, piv_l, inverse):
    cross = kernel_block(tx, piv_x, tsq, piv_sq) - jnp.dot(
        tl, piv_l.T, preferred_element_type=jnp.float32
    )
    return jnp.dot(
        cross, inverse.T, precision=lax.Precision.HIGHEST, preferred_element_type=jnp.float32
    ).astype(jnp.bfloat16)


def on_device(features, factors, pivots, owners):
    rows = features.shape[0]
    count = lax.axis_size(("blk", "grp"))
    width = features.shape[1]
    received = []
    for rnd in range(ROUNDS):
        picked = from_owner(features, factors, pivots[rnd], owners[rnd])
        wide = broadcast_sum(picked, bit_order(count))
        received.append((wide[:, :width], wide[:, width:]))
    shifted, _ = lax.optimization_barrier((features, received[-1][0]))
    carried = [passed_along(shifted, "blk", step) for step in (1, 2)]
    own_sq = squares(features)
    grand_total = jnp.sum(kernel_block(features, features, own_sq, own_sq), axis=1)
    for other in carried:
        grand_total = grand_total + jnp.sum(
            kernel_block(features, other, own_sq, squares(other)), axis=1
        )
    embedding = grand_total / (3.0 * rows)
    current = factors
    newcols = []
    blocks_x = []
    block_squared_norms = []
    block_factor_rows = []
    inverses = []
    for rnd in range(ROUNDS):
        piv_x, piv_l = received[rnd]
        piv_sq = squares(piv_x)
        for prior in range(rnd):
            extra = apply_block(
                piv_x,
                piv_sq,
                piv_l,
                blocks_x[prior],
                block_squared_norms[prior],
                block_factor_rows[prior],
                inverses[prior],
            )
            piv_l = jnp.concatenate([piv_l, extra], axis=1)
        inverses.append(solve_block(piv_x, piv_sq, piv_l))
        blocks_x.append(piv_x)
        block_squared_norms.append(piv_sq)
        block_factor_rows.append(piv_l)
    for rnd in range(ROUNDS):
        fresh = apply_block(
            features,
            own_sq,
            current,
            blocks_x[rnd],
            block_squared_norms[rnd],
            block_factor_rows[rnd],
            inverses[rnd],
        )
        newcols.append(fresh)
        current = jnp.concatenate([current, fresh], axis=1)
    columns = jnp.concatenate(newcols, axis=1)
    wide = current.astype(jnp.float32)
    leftover = 1.0 - jnp.sum(wide * wide, axis=1)
    return (embedding, columns, leftover)


def solution(mesh):
    placed = (P(("blk", "grp"), None), P(("blk", "grp"), None), P(), P())
    return jax.shard_map(
        on_device,
        mesh=mesh,
        in_specs=placed,
        out_specs=(P(("blk", "grp")), P(("blk", "grp"), None), P(("blk", "grp"))),
        check_vma=False,
    )
```

```python
import jax
import jax.numpy as jnp
from jax import lax
from jax.sharding import PartitionSpec as P

F = 2048
ROUNDS = 2


def passed_along(value, axis, steps):
    count = lax.axis_size(axis)
    pairs = [(source, (source + steps) % count) for source in range(count)]
    return lax.ppermute(value, axis, pairs)


def device_index():
    return lax.axis_index("blk") * lax.axis_size("grp") + lax.axis_index("grp")


def picked_rows(block, rows, take):
    selector = (rows[:, None] == jnp.arange(block.shape[0], dtype=rows.dtype)[None, :]) & take
    return jnp.dot(selector.astype(block.dtype), block, preferred_element_type=jnp.float32)


def from_owner(features, factors, rows, owner):
    take = device_index() == owner
    return jnp.concatenate(
        [picked_rows(features, rows, take), picked_rows(factors, rows, take)], axis=1
    ).astype(jnp.bfloat16)


def flip_pairs(bit, count):
    return [(source, source ^ (1 << bit)) for source in range(count)]


def broadcast_sum(value, order):
    axes = ("blk", "grp")
    count = lax.axis_size(axes)
    me = device_index()
    current = value
    for bit in order:
        half = current.shape[0] // 2
        upper = ((me >> bit) & 1) == 1
        keep = jnp.where(upper, current[half:], current[:half])
        send = jnp.where(upper, current[:half], current[half:])
        current = keep + lax.ppermute(send, axes, flip_pairs(bit, count))
    for bit in reversed(order):
        upper = ((me >> bit) & 1) == 1
        other = lax.ppermute(current, axes, flip_pairs(bit, count))
        current = jnp.where(
            upper, jnp.concatenate([other, current]), jnp.concatenate([current, other])
        )
    return current


def bit_order(count):
    bits = count.bit_length() - 1
    near = [0, 2, 3, 5, 1, 4, 6, 7]
    return [b for b in near if b < bits] + list(range(len(near), bits))


def squares(block):
    wide = block.astype(jnp.float32)
    return jnp.sum(wide * wide, axis=1)


def kernel_block(left, right, left_sq, right_sq):
    gram = jnp.dot(left, right.T, preferred_element_type=jnp.float32)
    dist = left_sq[:, None] + right_sq[None, :] - 2.0 * gram
    return jnp.exp(-dist / (8.0 * F))


def solve_block(piv_x, piv_sq, piv_l):
    schur = kernel_block(piv_x, piv_x, piv_sq, piv_sq) - jnp.dot(
        piv_l, piv_l.T, preferred_element_type=jnp.float32
    )
    lower = jnp.linalg.cholesky(schur)
    ident = jnp.eye(schur.shape[0], dtype=jnp.float32)
    return lax.linalg.triangular_solve(lower, ident, left_side=True, lower=True)


def apply_block(tx, tsq, tl, piv_x, piv_sq, piv_l, inverse):
    cross = kernel_block(tx, piv_x, tsq, piv_sq) - jnp.dot(
        tl, piv_l.T, preferred_element_type=jnp.float32
    )
    return jnp.dot(
        cross, inverse.T, precision=lax.Precision.HIGHEST, preferred_element_type=jnp.float32
    ).astype(jnp.bfloat16)


def on_device(features, factors, pivots, owners):
    rows = features.shape[0]
    count = lax.axis_size(("blk", "grp"))
    width = features.shape[1]
    received = []
    for rnd in range(ROUNDS):
        picked = from_owner(features, factors, pivots[rnd], owners[rnd])
        if received:
            picked, earlier = lax.optimization_barrier((picked, received[-1]))
            received[-1] = earlier
        wide = broadcast_sum(picked, bit_order(count))
        received.append((wide[:, :width], wide[:, width:]))
    shifted, _ = lax.optimization_barrier((features, received[-1][0]))
    carried = [passed_along(shifted, "blk", step) for step in (1, 2)]
    own_sq = squares(features)
    grand_total = jnp.sum(kernel_block(features, features, own_sq, own_sq), axis=1)
    for other in carried:
        grand_total = grand_total + jnp.sum(
            kernel_block(features, other, own_sq, squares(other)), axis=1
        )
    embedding = grand_total / (3.0 * rows)
    current = factors
    newcols = []
    blocks_x = []
    block_squared_norms = []
    block_factor_rows = []
    inverses = []
    for rnd in range(ROUNDS):
        piv_x, piv_l = received[rnd]
        piv_sq = squares(piv_x)
        for prior in range(rnd):
            extra = apply_block(
                piv_x,
                piv_sq,
                piv_l,
                blocks_x[prior],
                block_squared_norms[prior],
                block_factor_rows[prior],
                inverses[prior],
            )
            piv_l = jnp.concatenate([piv_l, extra], axis=1)
        inverses.append(solve_block(piv_x, piv_sq, piv_l))
        blocks_x.append(piv_x)
        block_squared_norms.append(piv_sq)
        block_factor_rows.append(piv_l)
    for rnd in range(ROUNDS):
        fresh = apply_block(
            features,
            own_sq,
            current,
            blocks_x[rnd],
            block_squared_norms[rnd],
            block_factor_rows[rnd],
            inverses[rnd],
        )
        newcols.append(fresh)
        current = jnp.concatenate([current, fresh], axis=1)
    columns = jnp.concatenate(newcols, axis=1)
    wide = current.astype(jnp.float32)
    leftover = 1.0 - jnp.sum(wide * wide, axis=1)
    return (embedding, columns, leftover)


def solution(mesh):
    placed = (P(("blk", "grp"), None), P(("blk", "grp"), None), P(), P())
    return jax.shard_map(
        on_device,
        mesh=mesh,
        in_specs=placed,
        out_specs=(P(("blk", "grp")), P(("blk", "grp"), None), P(("blk", "grp"))),
        check_vma=False,
    )
```

```python
import jax
import jax.numpy as jnp
from jax import lax
from jax.sharding import PartitionSpec as P

F = 2048
ROUNDS = 2


def passed_along(value, axis, steps):
    count = lax.axis_size(axis)
    pairs = [(source, (source + steps) % count) for source in range(count)]
    return lax.ppermute(value, axis, pairs)


def device_index():
    return lax.axis_index("blk") * lax.axis_size("grp") + lax.axis_index("grp")


def picked_rows(block, rows, take):
    selector = (rows[:, None] == jnp.arange(block.shape[0], dtype=rows.dtype)[None, :]) & take
    return jnp.dot(selector.astype(block.dtype), block, preferred_element_type=jnp.float32)


def from_owner(features, factors, rows, owner):
    take = device_index() == owner
    return jnp.concatenate(
        [picked_rows(features, rows, take), picked_rows(factors, rows, take)], axis=1
    ).astype(jnp.bfloat16)


def flip_pairs(bit, count):
    return [(source, source ^ (1 << bit)) for source in range(count)]


def broadcast_sum(value, order):
    axes = ("blk", "grp")
    count = lax.axis_size(axes)
    me = device_index()
    current = value
    for bit in order:
        half = current.shape[0] // 2
        upper = ((me >> bit) & 1) == 1
        keep = jnp.where(upper, current[half:], current[:half])
        send = jnp.where(upper, current[:half], current[half:])
        current = keep + lax.ppermute(send, axes, flip_pairs(bit, count))
    for bit in reversed(order):
        upper = ((me >> bit) & 1) == 1
        other = lax.ppermute(current, axes, flip_pairs(bit, count))
        current = jnp.where(
            upper, jnp.concatenate([other, current]), jnp.concatenate([current, other])
        )
    return current


def bit_order(count):
    bits = count.bit_length() - 1
    near = [0, 2, 3, 5, 1, 4, 6, 7]
    return [b for b in near if b < bits] + list(range(len(near), bits))


def squares(block):
    wide = block.astype(jnp.float32)
    return jnp.sum(wide * wide, axis=1)


def kernel_block(left, right, left_sq, right_sq):
    gram = jnp.dot(left, right.T, preferred_element_type=jnp.float32)
    dist = left_sq[:, None] + right_sq[None, :] - 2.0 * gram
    return jnp.exp(-dist / (8.0 * F))


def solve_block(piv_x, piv_sq, piv_l):
    schur = kernel_block(piv_x, piv_x, piv_sq, piv_sq) - jnp.dot(
        piv_l, piv_l.T, preferred_element_type=jnp.float32
    )
    lower = jnp.linalg.cholesky(schur)
    ident = jnp.eye(schur.shape[0], dtype=jnp.float32)
    return lax.linalg.triangular_solve(lower, ident, left_side=True, lower=True)


def apply_block(tx, tsq, tl, piv_x, piv_sq, piv_l, inverse):
    cross = kernel_block(tx, piv_x, tsq, piv_sq) - jnp.dot(
        tl, piv_l.T, preferred_element_type=jnp.float32
    )
    return jnp.dot(
        cross, inverse.T, precision=lax.Precision.HIGHEST, preferred_element_type=jnp.float32
    ).astype(jnp.bfloat16)


def on_device(features, factors, pivots, owners):
    rows = features.shape[0]
    count = lax.axis_size(("blk", "grp"))
    width = features.shape[1]
    picked = jnp.concatenate(
        [from_owner(features, factors, pivots[rnd], owners[rnd]) for rnd in range(ROUNDS)], axis=1
    )
    wide = broadcast_sum(picked, bit_order(count))
    features, factors, wide = lax.optimization_barrier((features, factors, wide))
    step = wide.shape[1] // ROUNDS
    received = [
        (wide[:, rnd * step : rnd * step + width], wide[:, rnd * step + width : (rnd + 1) * step])
        for rnd in range(ROUNDS)
    ]
    carried = [passed_along(features, "blk", step) for step in (1, 2)]
    own_sq = squares(features)
    grand_total = jnp.sum(kernel_block(features, features, own_sq, own_sq), axis=1)
    for other in carried:
        grand_total = grand_total + jnp.sum(
            kernel_block(features, other, own_sq, squares(other)), axis=1
        )
    embedding = grand_total / (3.0 * rows)
    current = factors
    newcols = []
    blocks_x = []
    block_squared_norms = []
    block_factor_rows = []
    inverses = []
    for rnd in range(ROUNDS):
        piv_x, piv_l = received[rnd]
        piv_sq = squares(piv_x)
        for prior in range(rnd):
            extra = apply_block(
                piv_x,
                piv_sq,
                piv_l,
                blocks_x[prior],
                block_squared_norms[prior],
                block_factor_rows[prior],
                inverses[prior],
            )
            piv_l = jnp.concatenate([piv_l, extra], axis=1)
        inverses.append(solve_block(piv_x, piv_sq, piv_l))
        blocks_x.append(piv_x)
        block_squared_norms.append(piv_sq)
        block_factor_rows.append(piv_l)
    for rnd in range(ROUNDS):
        fresh = apply_block(
            features,
            own_sq,
            current,
            blocks_x[rnd],
            block_squared_norms[rnd],
            block_factor_rows[rnd],
            inverses[rnd],
        )
        newcols.append(fresh)
        current = jnp.concatenate([current, fresh], axis=1)
    columns = jnp.concatenate(newcols, axis=1)
    wide = current.astype(jnp.float32)
    leftover = 1.0 - jnp.sum(wide * wide, axis=1)
    return (embedding, columns, leftover)


def solution(mesh):
    placed = (P(("blk", "grp"), None), P(("blk", "grp"), None), P(), P())
    return jax.shard_map(
        on_device,
        mesh=mesh,
        in_specs=placed,
        out_specs=(P(("blk", "grp")), P(("blk", "grp"), None), P(("blk", "grp"))),
        check_vma=False,
    )
```

```python
import jax
import jax.numpy as jnp
from jax import lax
from jax.sharding import PartitionSpec as P

F = 2048
ROUNDS = 2


def passed_along(value, axis, steps):
    count = lax.axis_size(axis)
    pairs = [(source, (source + steps) % count) for source in range(count)]
    return lax.ppermute(value, axis, pairs)


def device_index():
    return lax.axis_index("blk") * lax.axis_size("grp") + lax.axis_index("grp")


def picked_rows(block, rows, take):
    selector = (rows[:, None] == jnp.arange(block.shape[0], dtype=rows.dtype)[None, :]) & take
    return jnp.dot(selector.astype(block.dtype), block, preferred_element_type=jnp.float32)


def from_owner(features, factors, rows, owner):
    take = device_index() == owner
    return jnp.concatenate(
        [picked_rows(features, rows, take), picked_rows(factors, rows, take)], axis=1
    ).astype(jnp.bfloat16)


def flip_pairs(flip, count):
    return [(source, source ^ flip) for source in range(count)]


def broadcast_sum(value, digits):
    axes = ("blk", "grp")
    count = lax.axis_size(axes)
    me = device_index()

    def digit_of(low, high):
        return ((me >> low) & 1) + 2 * ((me >> high) & 1)

    def flip_of(m, low, high):
        return ((m & 1) << low) | ((m >> 1) << high)

    current = value
    for low, high in digits:
        part = current.shape[0] // 4
        mine = digit_of(low, high)
        keep = lax.dynamic_slice_in_dim(current, mine * part, part, 0)
        for m in (1, 2, 3):
            send = lax.dynamic_slice_in_dim(current, (mine ^ m) * part, part, 0)
            keep = keep + lax.ppermute(send, axes, flip_pairs(flip_of(m, low, high), count))
        current = keep
    for low, high in reversed(digits):
        part = current.shape[0]
        mine = digit_of(low, high)
        whole = jnp.zeros((4 * part,) + current.shape[1:], current.dtype)
        whole = lax.dynamic_update_slice_in_dim(whole, current, mine * part, 0)
        for m in (1, 2, 3):
            other = lax.ppermute(current, axes, flip_pairs(flip_of(m, low, high), count))
            whole = lax.dynamic_update_slice_in_dim(whole, other, (mine ^ m) * part, 0)
        current = whole
    return current


def bit_order(count):
    bits = count.bit_length() - 1
    near = [0, 2, 3, 5, 1, 4, 6, 7]
    order = [b for b in near if b < bits] + list(range(len(near), bits))
    return [(order[i], order[i + 1]) for i in range(0, len(order), 2)]


def squares(block):
    wide = block.astype(jnp.float32)
    return jnp.sum(wide * wide, axis=1)


def kernel_block(left, right, left_sq, right_sq):
    gram = jnp.dot(left, right.T, preferred_element_type=jnp.float32)
    dist = left_sq[:, None] + right_sq[None, :] - 2.0 * gram
    return jnp.exp(-dist / (8.0 * F))


def solve_block(piv_x, piv_sq, piv_l):
    schur = kernel_block(piv_x, piv_x, piv_sq, piv_sq) - jnp.dot(
        piv_l, piv_l.T, preferred_element_type=jnp.float32
    )
    lower = jnp.linalg.cholesky(schur)
    ident = jnp.eye(schur.shape[0], dtype=jnp.float32)
    return lax.linalg.triangular_solve(lower, ident, left_side=True, lower=True)


def apply_block(tx, tsq, tl, piv_x, piv_sq, piv_l, inverse):
    cross = kernel_block(tx, piv_x, tsq, piv_sq) - jnp.dot(
        tl, piv_l.T, preferred_element_type=jnp.float32
    )
    return jnp.dot(
        cross, inverse.T, precision=lax.Precision.HIGHEST, preferred_element_type=jnp.float32
    ).astype(jnp.bfloat16)


def on_device(features, factors, pivots, owners):
    rows = features.shape[0]
    count = lax.axis_size(("blk", "grp"))
    width = features.shape[1]
    picked = jnp.concatenate(
        [from_owner(features, factors, pivots[rnd], owners[rnd]) for rnd in range(ROUNDS)], axis=1
    )
    wide = broadcast_sum(picked, bit_order(count))
    features, factors, wide = lax.optimization_barrier((features, factors, wide))
    step = wide.shape[1] // ROUNDS
    received = [
        (wide[:, rnd * step : rnd * step + width], wide[:, rnd * step + width : (rnd + 1) * step])
        for rnd in range(ROUNDS)
    ]
    carried = [passed_along(features, "blk", step) for step in (1, 2)]
    own_sq = squares(features)
    grand_total = jnp.sum(kernel_block(features, features, own_sq, own_sq), axis=1)
    for other in carried:
        grand_total = grand_total + jnp.sum(
            kernel_block(features, other, own_sq, squares(other)), axis=1
        )
    embedding = grand_total / (3.0 * rows)
    current = factors
    newcols = []
    blocks_x = []
    block_squared_norms = []
    block_factor_rows = []
    inverses = []
    for rnd in range(ROUNDS):
        piv_x, piv_l = received[rnd]
        piv_sq = squares(piv_x)
        for prior in range(rnd):
            extra = apply_block(
                piv_x,
                piv_sq,
                piv_l,
                blocks_x[prior],
                block_squared_norms[prior],
                block_factor_rows[prior],
                inverses[prior],
            )
            piv_l = jnp.concatenate([piv_l, extra], axis=1)
        inverses.append(solve_block(piv_x, piv_sq, piv_l))
        blocks_x.append(piv_x)
        block_squared_norms.append(piv_sq)
        block_factor_rows.append(piv_l)
    for rnd in range(ROUNDS):
        fresh = apply_block(
            features,
            own_sq,
            current,
            blocks_x[rnd],
            block_squared_norms[rnd],
            block_factor_rows[rnd],
            inverses[rnd],
        )
        newcols.append(fresh)
        current = jnp.concatenate([current, fresh], axis=1)
    columns = jnp.concatenate(newcols, axis=1)
    wide = current.astype(jnp.float32)
    leftover = 1.0 - jnp.sum(wide * wide, axis=1)
    return (embedding, columns, leftover)


def solution(mesh):
    placed = (P(("blk", "grp"), None), P(("blk", "grp"), None), P(), P())
    return jax.shard_map(
        on_device,
        mesh=mesh,
        in_specs=placed,
        out_specs=(P(("blk", "grp")), P(("blk", "grp"), None), P(("blk", "grp"))),
        check_vma=False,
    )
```

```python
import jax
import jax.numpy as jnp
from jax import lax
from jax.sharding import PartitionSpec as P

F = 2048
ROUNDS = 2


def passed_along(value, axis, steps):
    count = lax.axis_size(axis)
    pairs = [(source, (source + steps) % count) for source in range(count)]
    return lax.ppermute(value, axis, pairs)


def device_index():
    return lax.axis_index("blk") * lax.axis_size("grp") + lax.axis_index("grp")


def picked_rows(block, rows, take):
    selector = (rows[:, None] == jnp.arange(block.shape[0], dtype=rows.dtype)[None, :]) & take
    return jnp.dot(selector.astype(block.dtype), block, preferred_element_type=jnp.float32)


def from_owner(features, factors, rows, owner):
    take = device_index() == owner
    return jnp.concatenate(
        [picked_rows(features, rows, take), picked_rows(factors, rows, take)], axis=1
    ).astype(jnp.bfloat16)


def flip_pairs(bit, count):
    return [(source, source ^ (1 << bit)) for source in range(count)]


def broadcast_sum(value, order):
    axes = ("blk", "grp")
    count = lax.axis_size(axes)
    me = device_index()
    current = value
    for bit in order:
        half = current.shape[0] // 2
        upper = ((me >> bit) & 1) == 1
        keep = jnp.where(upper, current[half:], current[:half])
        send = jnp.where(upper, current[:half], current[half:])
        current = keep + lax.ppermute(send, axes, flip_pairs(bit, count))
    for bit in reversed(order):
        upper = ((me >> bit) & 1) == 1
        other = lax.ppermute(current, axes, flip_pairs(bit, count))
        current = jnp.where(
            upper, jnp.concatenate([other, current]), jnp.concatenate([current, other])
        )
    return current


def bit_order(count):
    bits = count.bit_length() - 1
    near = [0, 2, 3, 5, 1, 4, 6, 7]
    return [b for b in near if b < bits] + list(range(len(near), bits))


def squares(block):
    wide = block.astype(jnp.float32)
    return jnp.sum(wide * wide, axis=1)


def kernel_block(left, right, left_sq, right_sq):
    gram = jnp.dot(left, right.T, preferred_element_type=jnp.float32)
    dist = left_sq[:, None] + right_sq[None, :] - 2.0 * gram
    return jnp.exp(-dist / (8.0 * F))


def solve_block(piv_x, piv_sq, piv_l):
    schur = kernel_block(piv_x, piv_x, piv_sq, piv_sq) - jnp.dot(
        piv_l, piv_l.T, preferred_element_type=jnp.float32
    )
    lower = jnp.linalg.cholesky(schur)
    ident = jnp.eye(schur.shape[0], dtype=jnp.float32)
    return lax.linalg.triangular_solve(lower, ident, left_side=True, lower=True)


def apply_block(tx, tsq, tl, piv_x, piv_sq, piv_l, inverse):
    cross = kernel_block(tx, piv_x, tsq, piv_sq) - jnp.dot(
        tl, piv_l.T, preferred_element_type=jnp.float32
    )
    return jnp.dot(
        cross, inverse.T, precision=lax.Precision.HIGHEST, preferred_element_type=jnp.float32
    ).astype(jnp.bfloat16)


def on_device(features, factors, pivots, owners):
    rows = features.shape[0]
    count = lax.axis_size(("blk", "grp"))
    width = features.shape[1]
    picked = jnp.concatenate(
        [from_owner(features, factors, pivots[rnd], owners[rnd]) for rnd in range(ROUNDS)], axis=1
    )
    wide = broadcast_sum(picked, bit_order(count))
    own_sq = squares(features)
    own_total = jnp.sum(kernel_block(features, features, own_sq, own_sq), axis=1)
    features, factors, wide = lax.optimization_barrier((features, factors, wide))
    step = wide.shape[1] // ROUNDS
    received = [
        (wide[:, rnd * step : rnd * step + width], wide[:, rnd * step + width : (rnd + 1) * step])
        for rnd in range(ROUNDS)
    ]
    carried = [passed_along(features, "blk", step) for step in (1, 2)]
    own_sq = squares(features)
    grand_total = own_total
    for other in carried:
        grand_total = grand_total + jnp.sum(
            kernel_block(features, other, own_sq, squares(other)), axis=1
        )
    embedding = grand_total / (3.0 * rows)
    current = factors
    newcols = []
    blocks_x = []
    block_squared_norms = []
    block_factor_rows = []
    inverses = []
    for rnd in range(ROUNDS):
        piv_x, piv_l = received[rnd]
        piv_sq = squares(piv_x)
        for prior in range(rnd):
            extra = apply_block(
                piv_x,
                piv_sq,
                piv_l,
                blocks_x[prior],
                block_squared_norms[prior],
                block_factor_rows[prior],
                inverses[prior],
            )
            piv_l = jnp.concatenate([piv_l, extra], axis=1)
        inverses.append(solve_block(piv_x, piv_sq, piv_l))
        blocks_x.append(piv_x)
        block_squared_norms.append(piv_sq)
        block_factor_rows.append(piv_l)
    for rnd in range(ROUNDS):
        fresh = apply_block(
            features,
            own_sq,
            current,
            blocks_x[rnd],
            block_squared_norms[rnd],
            block_factor_rows[rnd],
            inverses[rnd],
        )
        newcols.append(fresh)
        current = jnp.concatenate([current, fresh], axis=1)
    columns = jnp.concatenate(newcols, axis=1)
    wide = current.astype(jnp.float32)
    leftover = 1.0 - jnp.sum(wide * wide, axis=1)
    return (embedding, columns, leftover)


def solution(mesh):
    placed = (P(("blk", "grp"), None), P(("blk", "grp"), None), P(), P())
    return jax.shard_map(
        on_device,
        mesh=mesh,
        in_specs=placed,
        out_specs=(P(("blk", "grp")), P(("blk", "grp"), None), P(("blk", "grp"))),
        check_vma=False,
    )
```

```python
import jax
import jax.numpy as jnp
from jax import lax
from jax.sharding import PartitionSpec as P

F = 2048
ROUNDS = 2


def passed_along(value, axis, steps):
    count = lax.axis_size(axis)
    pairs = [(source, (source + steps) % count) for source in range(count)]
    return lax.ppermute(value, axis, pairs)


def device_index():
    return lax.axis_index("blk") * lax.axis_size("grp") + lax.axis_index("grp")


def picked_rows(block, rows, take):
    selector = (rows[:, None] == jnp.arange(block.shape[0], dtype=rows.dtype)[None, :]) & take
    return jnp.dot(selector.astype(block.dtype), block, preferred_element_type=jnp.float32)


def from_owner(features, factors, pivots, owners):
    rounds = pivots.shape[0]
    take = jnp.repeat(device_index() == owners, pivots.shape[1])[:, None]
    rows = pivots.reshape(-1)
    return jnp.concatenate(
        [picked_rows(features, rows, take), picked_rows(factors, rows, take)], axis=1
    ).astype(jnp.bfloat16)


def flip_pairs(bit, count):
    return [(source, source ^ (1 << bit)) for source in range(count)]


def broadcast_sum(value, order):
    axes = ("blk", "grp")
    count = lax.axis_size(axes)
    me = device_index()
    current = value
    for bit in order:
        half = current.shape[0] // 2
        upper = ((me >> bit) & 1) == 1
        keep = jnp.where(upper, current[half:], current[:half])
        send = jnp.where(upper, current[:half], current[half:])
        current = keep + lax.ppermute(send, axes, flip_pairs(bit, count))
    for bit in reversed(order):
        upper = ((me >> bit) & 1) == 1
        other = lax.ppermute(current, axes, flip_pairs(bit, count))
        current = jnp.where(
            upper, jnp.concatenate([other, current]), jnp.concatenate([current, other])
        )
    return current


def bit_orders(count):
    bits = count.bit_length() - 1
    orders = []
    for near in ([0, 2, 3, 5, 1, 4, 6, 7], [0, 3, 5, 2, 4, 1, 7, 6]):
        orders.append([b for b in near if b < bits] + list(range(len(near), bits)))
    return orders


def squares(block):
    wide = block.astype(jnp.float32)
    return jnp.sum(wide * wide, axis=1)


def kernel_block(left, right, left_sq, right_sq):
    gram = jnp.dot(left, right.T, preferred_element_type=jnp.float32)
    dist = left_sq[:, None] + right_sq[None, :] - 2.0 * gram
    return jnp.exp(-dist / (8.0 * F))


def solve_block(piv_x, piv_sq, piv_l):
    schur = kernel_block(piv_x, piv_x, piv_sq, piv_sq) - jnp.dot(
        piv_l, piv_l.T, preferred_element_type=jnp.float32
    )
    lower = jnp.linalg.cholesky(schur)
    ident = jnp.eye(schur.shape[0], dtype=jnp.float32)
    return lax.linalg.triangular_solve(lower, ident, left_side=True, lower=True)


def apply_block(tx, tsq, tl, piv_x, piv_sq, piv_l, inverse):
    cross = kernel_block(tx, piv_x, tsq, piv_sq) - jnp.dot(
        tl, piv_l.T, preferred_element_type=jnp.float32
    )
    return jnp.dot(
        cross, inverse.T, precision=lax.Precision.HIGHEST, preferred_element_type=jnp.float32
    ).astype(jnp.bfloat16)


def on_device(features, factors, pivots, owners):
    rows = features.shape[0]
    count = lax.axis_size(("blk", "grp"))
    width = features.shape[1]
    picked = from_owner(features, factors, pivots, owners)
    split = picked.shape[1] // 2
    first, second = bit_orders(count)
    wide = jnp.concatenate(
        [broadcast_sum(picked[:, :split], first), broadcast_sum(picked[:, split:], second)], axis=1
    )
    features, factors, wide = lax.optimization_barrier((features, factors, wide))
    size = pivots.shape[1]
    received = [
        (wide[rnd * size : (rnd + 1) * size, :width], wide[rnd * size : (rnd + 1) * size, width:])
        for rnd in range(ROUNDS)
    ]
    carried = [passed_along(features, "blk", step) for step in (1, 2)]
    own_sq = squares(features)
    grand_total = jnp.sum(kernel_block(features, features, own_sq, own_sq), axis=1)
    for other in carried:
        grand_total = grand_total + jnp.sum(
            kernel_block(features, other, own_sq, squares(other)), axis=1
        )
    embedding = grand_total / (3.0 * rows)
    current = factors
    newcols = []
    blocks_x = []
    block_squared_norms = []
    block_factor_rows = []
    inverses = []
    for rnd in range(ROUNDS):
        piv_x, piv_l = received[rnd]
        piv_sq = squares(piv_x)
        for prior in range(rnd):
            extra = apply_block(
                piv_x,
                piv_sq,
                piv_l,
                blocks_x[prior],
                block_squared_norms[prior],
                block_factor_rows[prior],
                inverses[prior],
            )
            piv_l = jnp.concatenate([piv_l, extra], axis=1)
        inverses.append(solve_block(piv_x, piv_sq, piv_l))
        blocks_x.append(piv_x)
        block_squared_norms.append(piv_sq)
        block_factor_rows.append(piv_l)
    for rnd in range(ROUNDS):
        fresh = apply_block(
            features,
            own_sq,
            current,
            blocks_x[rnd],
            block_squared_norms[rnd],
            block_factor_rows[rnd],
            inverses[rnd],
        )
        newcols.append(fresh)
        current = jnp.concatenate([current, fresh], axis=1)
    columns = jnp.concatenate(newcols, axis=1)
    wide = current.astype(jnp.float32)
    leftover = 1.0 - jnp.sum(wide * wide, axis=1)
    return (embedding, columns, leftover)


def solution(mesh):
    placed = (P(("blk", "grp"), None), P(("blk", "grp"), None), P(), P())
    return jax.shard_map(
        on_device,
        mesh=mesh,
        in_specs=placed,
        out_specs=(P(("blk", "grp")), P(("blk", "grp"), None), P(("blk", "grp"))),
        check_vma=False,
    )
```

```python
import jax
import jax.numpy as jnp
from jax import lax
from jax.sharding import PartitionSpec as P

F = 2048
ROUNDS = 2


def passed_along(value, axis, steps):
    count = lax.axis_size(axis)
    pairs = [(source, (source + steps) % count) for source in range(count)]
    return lax.ppermute(value, axis, pairs)


def device_index():
    return lax.axis_index("blk") * lax.axis_size("grp") + lax.axis_index("grp")


def picked_rows(block, rows, take):
    selector = (rows[:, None] == jnp.arange(block.shape[0], dtype=rows.dtype)[None, :]) & take
    return jnp.dot(selector.astype(block.dtype), block, preferred_element_type=jnp.float32)


def from_owner(features, factors, pivots, owners):
    rounds = pivots.shape[0]
    take = jnp.repeat(device_index() == owners, pivots.shape[1])[:, None]
    rows = pivots.reshape(-1)
    return jnp.concatenate(
        [picked_rows(features, rows, take), picked_rows(factors, rows, take)], axis=1
    ).astype(jnp.bfloat16)


def flip_pairs(bit, count):
    return [(source, source ^ (1 << bit)) for source in range(count)]


def broadcast_sum(value, order):
    axes = ("blk", "grp")
    count = lax.axis_size(axes)
    me = device_index()
    current = value
    for bit in order:
        half = current.shape[0] // 2
        upper = ((me >> bit) & 1) == 1
        keep = jnp.where(upper, current[half:], current[:half])
        send = jnp.where(upper, current[:half], current[half:])
        current = keep + lax.ppermute(send, axes, flip_pairs(bit, count))
    for bit in reversed(order):
        upper = ((me >> bit) & 1) == 1
        other = lax.ppermute(current, axes, flip_pairs(bit, count))
        current = jnp.where(
            upper, jnp.concatenate([other, current]), jnp.concatenate([current, other])
        )
    return current


def bit_orders(count):
    bits = count.bit_length() - 1
    orders = []
    for near in ([0, 2, 3, 5, 1, 4, 6, 7], [0, 3, 5, 2, 4, 1, 7, 6]):
        orders.append([b for b in near if b < bits] + list(range(len(near), bits)))
    return orders


def squares(block):
    wide = block.astype(jnp.float32)
    return jnp.sum(wide * wide, axis=1)


def kernel_block(left, right, left_sq, right_sq):
    gram = jnp.dot(left, right.T, preferred_element_type=jnp.float32)
    dist = left_sq[:, None] + right_sq[None, :] - 2.0 * gram
    return jnp.exp(-dist / (8.0 * F))


def solve_block(piv_x, piv_sq, piv_l):
    schur = kernel_block(piv_x, piv_x, piv_sq, piv_sq) - jnp.dot(
        piv_l, piv_l.T, preferred_element_type=jnp.float32
    )
    lower = jnp.linalg.cholesky(schur)
    ident = jnp.eye(schur.shape[0], dtype=jnp.float32)
    return lax.linalg.triangular_solve(lower, ident, left_side=True, lower=True)


def apply_block(tx, tsq, tl, piv_x, piv_sq, piv_l, inverse):
    cross = kernel_block(tx, piv_x, tsq, piv_sq) - jnp.dot(
        tl, piv_l.T, preferred_element_type=jnp.float32
    )
    return jnp.dot(
        cross, inverse.T, precision=lax.Precision.HIGHEST, preferred_element_type=jnp.float32
    ).astype(jnp.bfloat16)


def on_device(features, factors, pivots, owners):
    rows = features.shape[0]
    count = lax.axis_size(("blk", "grp"))
    width = features.shape[1]
    picked = from_owner(features, factors, pivots, owners)
    split = picked.shape[1] // 2
    first, second = bit_orders(count)
    wide = jnp.concatenate(
        [broadcast_sum(picked[:, :split], first), broadcast_sum(picked[:, split:], second)], axis=1
    )
    features, factors, wide = lax.optimization_barrier((features, factors, wide))
    size = pivots.shape[1]
    received = [
        (wide[rnd * size : (rnd + 1) * size, :width], wide[rnd * size : (rnd + 1) * size, width:])
        for rnd in range(ROUNDS)
    ]
    own_sq = squares(features)
    carried = [passed_along((features, own_sq), "blk", step) for step in (1, 2)]
    grand_total = jnp.sum(kernel_block(features, features, own_sq, own_sq), axis=1)
    for other, other_sq in carried:
        grand_total = grand_total + jnp.sum(
            kernel_block(features, other, own_sq, other_sq), axis=1
        )
    embedding = grand_total / (3.0 * rows)
    current = factors
    newcols = []
    blocks_x = []
    block_squared_norms = []
    block_factor_rows = []
    inverses = []
    for rnd in range(ROUNDS):
        piv_x, piv_l = received[rnd]
        piv_sq = squares(piv_x)
        for prior in range(rnd):
            extra = apply_block(
                piv_x,
                piv_sq,
                piv_l,
                blocks_x[prior],
                block_squared_norms[prior],
                block_factor_rows[prior],
                inverses[prior],
            )
            piv_l = jnp.concatenate([piv_l, extra], axis=1)
        inverses.append(solve_block(piv_x, piv_sq, piv_l))
        blocks_x.append(piv_x)
        block_squared_norms.append(piv_sq)
        block_factor_rows.append(piv_l)
    for rnd in range(ROUNDS):
        fresh = apply_block(
            features,
            own_sq,
            current,
            blocks_x[rnd],
            block_squared_norms[rnd],
            block_factor_rows[rnd],
            inverses[rnd],
        )
        newcols.append(fresh)
        current = jnp.concatenate([current, fresh], axis=1)
    columns = jnp.concatenate(newcols, axis=1)
    wide = current.astype(jnp.float32)
    leftover = 1.0 - jnp.sum(wide * wide, axis=1)
    return (embedding, columns, leftover)


def solution(mesh):
    placed = (P(("blk", "grp"), None), P(("blk", "grp"), None), P(), P())
    return jax.shard_map(
        on_device,
        mesh=mesh,
        in_specs=placed,
        out_specs=(P(("blk", "grp")), P(("blk", "grp"), None), P(("blk", "grp"))),
        check_vma=False,
    )
```

```python
import jax
import jax.numpy as jnp
from jax import lax
from jax.sharding import PartitionSpec as P

F = 2048
ROUNDS = 2


def passed_along(value, axis, steps):
    count = lax.axis_size(axis)
    pairs = [(source, (source + steps) % count) for source in range(count)]
    return lax.ppermute(value, axis, pairs)


def device_index():
    return lax.axis_index("blk") * lax.axis_size("grp") + lax.axis_index("grp")


def picked_rows(block, rows, take):
    selector = (rows[:, None] == jnp.arange(block.shape[0], dtype=rows.dtype)[None, :]) & take
    return jnp.dot(selector.astype(block.dtype), block, preferred_element_type=jnp.float32)


def from_owner(features, factors, pivots, owners):
    rounds = pivots.shape[0]
    take = jnp.repeat(device_index() == owners, pivots.shape[1])[:, None]
    rows = pivots.reshape(-1)
    return jnp.concatenate(
        [picked_rows(features, rows, take), picked_rows(factors, rows, take)], axis=1
    ).astype(jnp.bfloat16)


def flip_pairs(bit, count):
    return [(source, source ^ (1 << bit)) for source in range(count)]


def broadcast_sum(value, order):
    axes = ("blk", "grp")
    count = lax.axis_size(axes)
    me = device_index()
    current = value
    for bit in order:
        half = current.shape[0] // 2
        upper = ((me >> bit) & 1) == 1
        keep = jnp.where(upper, current[half:], current[:half])
        send = jnp.where(upper, current[:half], current[half:])
        current = keep + lax.ppermute(send, axes, flip_pairs(bit, count))
    for bit in reversed(order):
        upper = ((me >> bit) & 1) == 1
        other = lax.ppermute(current, axes, flip_pairs(bit, count))
        current = jnp.where(
            upper, jnp.concatenate([other, current]), jnp.concatenate([current, other])
        )
    return current


def bit_orders(count):
    bits = count.bit_length() - 1
    orders = []
    for near in ([0, 2, 3, 5, 1, 4, 6, 7], [0, 3, 5, 2, 4, 1, 7, 6], [0, 5, 2, 3, 6, 4, 1, 7]):
        orders.append([b for b in near if b < bits] + list(range(len(near), bits)))
    return orders


def squares(block):
    wide = block.astype(jnp.float32)
    return jnp.sum(wide * wide, axis=1)


def kernel_block(left, right, left_sq, right_sq):
    gram = jnp.dot(left, right.T, preferred_element_type=jnp.float32)
    dist = left_sq[:, None] + right_sq[None, :] - 2.0 * gram
    return jnp.exp(-dist / (8.0 * F))


def solve_block(piv_x, piv_sq, piv_l):
    schur = kernel_block(piv_x, piv_x, piv_sq, piv_sq) - jnp.dot(
        piv_l, piv_l.T, preferred_element_type=jnp.float32
    )
    lower = jnp.linalg.cholesky(schur)
    ident = jnp.eye(schur.shape[0], dtype=jnp.float32)
    return lax.linalg.triangular_solve(lower, ident, left_side=True, lower=True)


def apply_block(tx, tsq, tl, piv_x, piv_sq, piv_l, inverse):
    cross = kernel_block(tx, piv_x, tsq, piv_sq) - jnp.dot(
        tl, piv_l.T, preferred_element_type=jnp.float32
    )
    return jnp.dot(
        cross, inverse.T, precision=lax.Precision.HIGHEST, preferred_element_type=jnp.float32
    ).astype(jnp.bfloat16)


def on_device(features, factors, pivots, owners):
    rows = features.shape[0]
    count = lax.axis_size(("blk", "grp"))
    width = features.shape[1]
    picked = from_owner(features, factors, pivots, owners)
    orders = bit_orders(count)
    lanes = picked.shape[1] // 128
    edges = [128 * (lanes * k // len(orders)) for k in range(len(orders) + 1)]
    wide = jnp.concatenate(
        [
            broadcast_sum(picked[:, edges[k] : edges[k + 1]], order)
            for k, order in enumerate(orders)
        ],
        axis=1,
    )
    features, factors, wide = lax.optimization_barrier((features, factors, wide))
    size = pivots.shape[1]
    received = [
        (wide[rnd * size : (rnd + 1) * size, :width], wide[rnd * size : (rnd + 1) * size, width:])
        for rnd in range(ROUNDS)
    ]
    own_sq = squares(features)
    carried = [passed_along((features, own_sq), "blk", step) for step in (1, 2)]
    grand_total = jnp.sum(kernel_block(features, features, own_sq, own_sq), axis=1)
    for other, other_sq in carried:
        grand_total = grand_total + jnp.sum(
            kernel_block(features, other, own_sq, other_sq), axis=1
        )
    embedding = grand_total / (3.0 * rows)
    current = factors
    newcols = []
    blocks_x = []
    block_squared_norms = []
    block_factor_rows = []
    inverses = []
    for rnd in range(ROUNDS):
        piv_x, piv_l = received[rnd]
        piv_sq = squares(piv_x)
        for prior in range(rnd):
            extra = apply_block(
                piv_x,
                piv_sq,
                piv_l,
                blocks_x[prior],
                block_squared_norms[prior],
                block_factor_rows[prior],
                inverses[prior],
            )
            piv_l = jnp.concatenate([piv_l, extra], axis=1)
        inverses.append(solve_block(piv_x, piv_sq, piv_l))
        blocks_x.append(piv_x)
        block_squared_norms.append(piv_sq)
        block_factor_rows.append(piv_l)
    for rnd in range(ROUNDS):
        fresh = apply_block(
            features,
            own_sq,
            current,
            blocks_x[rnd],
            block_squared_norms[rnd],
            block_factor_rows[rnd],
            inverses[rnd],
        )
        newcols.append(fresh)
        current = jnp.concatenate([current, fresh], axis=1)
    columns = jnp.concatenate(newcols, axis=1)
    wide = current.astype(jnp.float32)
    leftover = 1.0 - jnp.sum(wide * wide, axis=1)
    return (embedding, columns, leftover)


def solution(mesh):
    placed = (P(("blk", "grp"), None), P(("blk", "grp"), None), P(), P())
    return jax.shard_map(
        on_device,
        mesh=mesh,
        in_specs=placed,
        out_specs=(P(("blk", "grp")), P(("blk", "grp"), None), P(("blk", "grp"))),
        check_vma=False,
    )
```
